256 devices in a mesh: row: 16 (over z, x_lo), col: 4 (over x_hi, core), layer: 4 (over y).
Axes of the slice: x: 4 (x_hi: 2, x_lo: 2; x = x_hi * 2 + x_lo), y: 4, z: 8, core: 2. Of those that a mesh axis runs over, the one named last changes fastest.
Arguments:
- density: bfloat16 [512, 16, 128, 128], P('row', 'col'), may hold values from -0.59765625 to 0.59765625
- block_offset: int32 [512, 16], P('row', 'col'), may hold values from 0 to 1, as said below
- filter_offset: int32 [64, 32], P('row', 'col'), may hold values from 0 to 3, as said below
- position: int32 [32], replicated, may hold values from 0 to 31, each once
Outputs:
- purified: float32 [64, 32, 128, 128], P(('row', 'layer'), 'col')
The draws below stay inside these ranges and needn't reach their ends.
Inputs may be any that keep to these rules, and one draw needn't show every extreme that they name: `block_offset`: slots fall into groups of 1 consecutive slots; within each group of a block row the offsets rise strictly (a group of one slot holds a single offset). `filter_offset`: slots fall into groups of 2 consecutive slots; within each group of a row the offsets rise strictly (a group of one slot holds a single offset).
All inputs are finite; a program needn't handle non-finite values.
Results may differ from the reference program's by a relative error of at most 0.0027.
Values may be sent and summed in bfloat16 or wider, within the bound.
No kernel may reach another device: no remote copies, remote signals or barrier semaphores. Data moves between devices by JAX's collectives and lax.ppermute only.
A program may use at most 128 MiB of HBM per device.

```python
import jax
import jax.numpy as jnp
from jax import lax

BS = 128
NB = 512
W = 16
WF = 32
RA = 4
RB = 32
WK = 1
WFK = 2
RS = 64
N_ROW = 16


def rising_offsets(key, rows, groups, per_group):
    gaps = jax.random.randint(key, (rows, groups, per_group), 1, 3, dtype=jnp.int32)
    return (jnp.cumsum(gaps, axis=-1) - 1).reshape(rows, groups * per_group).astype(jnp.int32)


def draw_block_offset(key, part):
    return rising_offsets(key, NB, W // WK, WK)


def draw_filter_offset(key, part):
    return rising_offsets(key, RS, WF // WFK, WFK)


def levels(own_key, dims, split, least, high):
    def one(axis_at, parts):
        draws = jax.random.uniform(jax.random.fold_in(jax.random.fold_in(own_key, 6), axis_at), (parts,), jnp.float32, least / len(split), high / len(split))
        return jnp.repeat(jnp.exp(draws), dims[axis_at] // parts).reshape((-1,) + (1,) * (len(dims) - axis_at - 1))

    gain = one(*split[0])
    for cut in split[1:]:
        gain = gain * one(*cut)
    return gain


def centred(rng, shape, width, bound, split=(), held_as=jnp.bfloat16):
    level = levels(rng, shape, split, -0.22, 0.18) if split else 1.0
    entries = jax.random.normal(rng, shape, jnp.float32) * width * level
    return jnp.minimum(jnp.maximum(entries, -bound), bound).astype(held_as)


def setup_inputs(seed: int = 0) -> dict:
    splits = jax.random.split(jax.random.key(seed), 5)
    density = centred(splits[0], (NB, W, BS, BS), 0.1, 0.59765625, ((0, 16), (1, 4)))
    block_offset = draw_block_offset(jax.random.fold_in(splits[4], 71), 0)
    filter_offset = draw_filter_offset(jax.random.fold_in(splits[4], 71), 0)
    position = jax.random.permutation(splits[3], NB // N_ROW).astype(jnp.int32)
    return dict(density=density, block_offset=block_offset, filter_offset=filter_offset, position=position)


def column_index(offsets, local_rows, position, image_of, group_size):
    extent = position.shape[0]
    groups = (jnp.arange(offsets.shape[1], dtype=jnp.int32) // group_size) * extent
    physical = (position[local_rows][:, None] + offsets) % extent
    return groups[None, :] + image_of[physical]


def row_product(density, block_column, left_blocks, left_columns, targets):
    right_blocks = density[left_columns].astype(jnp.float32)
    right_columns = block_column[left_columns]
    matches = (right_columns[None, :, :] == targets[:, None, None]).astype(jnp.float32)
    products = jnp.einsum("sxy,styz->stxz", left_blocks.astype(jnp.float32), right_blocks, precision=lax.Precision.HIGHEST)
    return jnp.einsum("ust,stxz->uxz", matches, products, precision=lax.Precision.HIGHEST)


def reference(density, block_offset, filter_offset, position):
    image_of = jnp.zeros((RB,), jnp.int32).at[position].set(jnp.arange(RB, dtype=jnp.int32))
    block_column = column_index(block_offset, jnp.arange(NB, dtype=jnp.int32) % RB, position, image_of, WK)
    slab = jnp.arange(RS, dtype=jnp.int32)
    slab_rows = ((slab // RA) * RB + slab % RA).astype(jnp.int32)
    filter_column = column_index(filter_offset, (slab % RA).astype(jnp.int32), position, image_of, WFK)

    def each_row(inputs):
        return row_product(density, block_column, inputs[0], inputs[1], inputs[2])

    square = lax.map(each_row, (density[slab_rows], block_column[slab_rows], filter_column))
    square_half = square.astype(jnp.bfloat16)
    cube = lax.map(each_row, (square_half, filter_column, filter_column))
    return 3.0 * square - 2.0 * cube
```

```python
import jax
import jax.numpy as jnp
from jax import lax
from jax.sharding import PartitionSpec as P

CANDIDATES = 4


def on_device(density, block_offset, filter_offset, position):
    extent = position.shape[0]
    slots_tile = density.shape[1]
    col_id = lax.axis_index("col")
    layer_id = lax.axis_index("layer")
    image_of = jnp.zeros((extent,), jnp.int32).at[position].set(jnp.arange(extent, dtype=jnp.int32))
    base = position[layer_id]
    ks = jnp.arange(CANDIDATES, dtype=jnp.int32)
    cand = image_of[(base + ks) % extent]

    picked = density[cand]
    picked_offsets = block_offset[cand]
    gathered = lax.all_gather(picked, "row", axis=0, tiled=False)
    gathered_offsets = lax.all_gather(picked_offsets, "row", axis=0, tiled=False)

    left = lax.all_gather(density[layer_id], "col", axis=0, tiled=True)
    own_ints = jnp.concatenate([block_offset[layer_id], filter_offset[layer_id]])
    all_ints = lax.all_gather(own_ints, "col", axis=0, tiled=False)
    left_offsets = all_ints[:, :slots_tile].reshape(-1)
    filter_all = all_ints[:, slots_tile:].reshape(-1)

    t_count = slots_tile
    groups = col_id * slots_tile + jnp.arange(t_count, dtype=jnp.int32)
    filter_own = filter_offset[layer_id].reshape(t_count, -1)
    target = groups[:, None] * extent + image_of[(base + filter_own) % extent]

    def right_columns(w_index, k_index):
        offsets = gathered_offsets[w_index, k_index]
        physical = (position[cand[k_index]][:, None] + offsets) % extent
        return groups[None, :] * extent + image_of[physical]

    row_groups = left.shape[0]
    w_all = jnp.arange(row_groups, dtype=jnp.int32)
    square_k = left_offsets
    square_right = gathered[w_all, square_k]
    square_match = right_columns(w_all, square_k)[:, :, None] == target[None, :, :]
    square_parts = jnp.einsum("wxy,wtyz->wtxz", left, square_right, preferred_element_type=jnp.float32)
    square = jnp.sum(
        jnp.where(square_match[:, :, :, None, None], square_parts[:, :, None], 0.0), axis=0
    )

    square_half = square.astype(jnp.bfloat16).reshape(-1, *square.shape[2:])
    square_all = lax.all_gather(square_half, "col", axis=0, tiled=True)

    v_all = jnp.arange(square_all.shape[0], dtype=jnp.int32)
    cube_w = v_all // (square_all.shape[0] // row_groups)
    cube_right = gathered[cube_w, filter_all]
    cube_match = right_columns(cube_w, filter_all)[:, :, None] == target[None, :, :]
    cube_parts = jnp.einsum("vxy,vtyz->vtxz", square_all, cube_right, preferred_element_type=jnp.float32)
    cube = jnp.sum(jnp.where(cube_match[:, :, :, None, None], cube_parts[:, :, None], 0.0), axis=0)

    result = 3.0 * square - 2.0 * cube
    return result.reshape(1, -1, *result.shape[2:])


def solution(mesh):
    placed = (P("row", "col", None, None), P("row", "col"), P("row", "col"), P())
    return jax.shard_map(
        on_device,
        mesh=mesh,
        in_specs=placed,
        out_specs=P(("row", "layer"), "col", None, None),
        check_vma=False,
    )
```

```python
import jax
import jax.numpy as jnp
from jax import lax
from jax.sharding import PartitionSpec as P

CANDIDATES = 4


def shifted(value, axis, steps):
    count = lax.axis_size(axis)
    pairs = [(source, (source + steps) % count) for source in range(count)]
    return lax.ppermute(value, axis, pairs)


def partner(value, axis):
    count = lax.axis_size(axis)
    return lax.ppermute(value, axis, [(source, source ^ 1) for source in range(count)])


def gather_rows(pair):
    row_count = lax.axis_size("row")
    z_count = row_count // 2
    row_id = lax.axis_index("row")
    z_id = row_id // 2
    x_lo = row_id % 2
    mine = pair
    theirs = partner(pair, "row")
    chunk = tuple(jnp.stack([a, b]) for a, b in zip(mine, theirs))

    def groups_of(z_source):
        z_source = z_source % z_count
        return [2 * z_source + x_lo, 2 * z_source + 1 - x_lo]

    pieces = [chunk]
    owners = groups_of(z_id)
    ahead, behind = chunk, chunk
    for distance in range(1, z_count // 2):
        ahead = shifted(ahead, "row", 2)
        behind = shifted(behind, "row", -2)
        pieces += [ahead, behind]
        owners += groups_of(z_id - distance) + groups_of(z_id + distance)
    last_ahead = shifted(tuple(a[:1] for a in ahead), "row", 2)
    last_behind = shifted(tuple(b[1:] for b in behind), "row", -2)
    pieces += [last_ahead, last_behind]
    owners += groups_of(z_id - z_count // 2)[:1] + groups_of(z_id + z_count // 2)[1:]
    data = jnp.concatenate([p[0] for p in pieces])
    offsets = jnp.concatenate([p[1] for p in pieces])
    owners = jnp.stack(owners).astype(jnp.int32) % row_count
    slot_of = jnp.zeros((row_count,), jnp.int32).at[owners].set(jnp.arange(row_count, dtype=jnp.int32))
    return data, offsets, slot_of


def gather_col(value):
    count = lax.axis_size("col")
    return jnp.stack([value] + [shifted(value, "col", d) for d in range(1, count)])


def on_device(density, block_offset, filter_offset, position):
    extent = position.shape[0]
    slots_tile = density.shape[1]
    col_count = lax.axis_size("col")
    col_id = lax.axis_index("col")
    layer_id = lax.axis_index("layer")
    image_of = jnp.zeros((extent,), jnp.int32).at[position].set(jnp.arange(extent, dtype=jnp.int32))
    base = position[layer_id]
    ks = jnp.arange(CANDIDATES, dtype=jnp.int32)
    cand = image_of[(base + ks) % extent]

    gathered, gathered_offsets, slot_of = gather_rows((density[cand], block_offset[cand]))

    col_of_piece = (col_id - jnp.arange(col_count, dtype=jnp.int32)) % col_count
    left = gather_col(density[layer_id]).reshape(-1, *density.shape[2:])
    own_ints = jnp.concatenate([block_offset[layer_id], filter_offset[layer_id]])
    all_ints = gather_col(own_ints)
    left_offsets = all_ints[:, :slots_tile].reshape(-1)
    filter_all = all_ints[:, slots_tile:].reshape(-1)
    left_w = (col_of_piece[:, None] * slots_tile + jnp.arange(slots_tile, dtype=jnp.int32)).reshape(-1)

    t_count = slots_tile
    groups = col_id * slots_tile + jnp.arange(t_count, dtype=jnp.int32)
    filter_own = filter_offset[layer_id].reshape(t_count, -1)
    target = groups[:, None] * extent + image_of[(base + filter_own) % extent]

    def right_columns(slot_index, k_index):
        offsets = gathered_offsets[slot_index, k_index]
        physical = (position[cand[k_index]][:, None] + offsets) % extent
        return groups[None, :] * extent + image_of[physical]

    square_slot = slot_of[left_w]
    square_right = gathered[square_slot, left_offsets]
    square_match = right_columns(square_slot, left_offsets)[:, :, None] == target[None, :, :]
    square_parts = jnp.einsum("wxy,wtyz->wtxz", left, square_right, preferred_element_type=jnp.float32)
    square = jnp.sum(
        jnp.where(square_match[:, :, :, None, None], square_parts[:, :, None], 0.0), axis=0
    )

    square_half = square.astype(jnp.bfloat16).reshape(-1, *square.shape[2:])
    per_col = square_half.shape[0]
    square_all = gather_col(square_half).reshape(-1, *square_half.shape[1:])
    v_all = (col_of_piece[:, None] * per_col + jnp.arange(per_col, dtype=jnp.int32)).reshape(-1)
    row_groups = slot_of.shape[0]
    cube_slot = slot_of[v_all // (col_count * per_col // row_groups)]
    cube_right = gathered[cube_slot, filter_all]
    cube_match = right_columns(cube_slot, filter_all)[:, :, None] == target[None, :, :]
    cube_parts = jnp.einsum("vxy,vtyz->vtxz", square_all, cube_right, preferred_element_type=jnp.float32)
    cube = jnp.sum(jnp.where(cube_match[:, :, :, None, None], cube_parts[:, :, None], 0.0), axis=0)

    result = 3.0 * square - 2.0 * cube
    return result.reshape(1, -1, *result.shape[2:])


def solution(mesh):
    placed = (P("row", "col", None, None), P("row", "col"), P("row", "col"), P())
    return jax.shard_map(
        on_device,
        mesh=mesh,
        in_specs=placed,
        out_specs=P(("row", "layer"), "col", None, None),
        check_vma=False,
    )
```

```python
import jax
import jax.numpy as jnp
from jax import lax
from jax.sharding import PartitionSpec as P

CANDIDATES = 4


def shifted(value, axis, steps):
    count = lax.axis_size(axis)
    pairs = [(source, (source + steps) % count) for source in range(count)]
    return lax.ppermute(value, axis, pairs)


def partner(value, axis):
    count = lax.axis_size(axis)
    return lax.ppermute(value, axis, [(source, source ^ 1) for source in range(count)])


def gather_rows(pair):
    row_count = lax.axis_size("row")
    z_count = row_count // 2
    row_id = lax.axis_index("row")
    z_id = row_id // 2
    x_lo = row_id % 2
    chunk = jnp.stack([pair, partner(pair, "row")])

    def groups_of(z_source):
        z_source = z_source % z_count
        return [2 * z_source + x_lo, 2 * z_source + 1 - x_lo]

    pieces = [chunk]
    owners = groups_of(z_id)
    ahead, behind = chunk, chunk
    for distance in range(1, z_count // 2):
        ahead = shifted(ahead, "row", 2)
        behind = shifted(behind, "row", -2)
        pieces += [ahead, behind]
        owners += groups_of(z_id - distance) + groups_of(z_id + distance)
    last_ahead = shifted(ahead[:1], "row", 2)
    last_behind = shifted(behind[1:], "row", -2)
    pieces += [last_ahead, last_behind]
    owners += groups_of(z_id - z_count // 2)[:1] + groups_of(z_id + z_count // 2)[1:]
    data = jnp.concatenate(pieces)
    owners = jnp.stack(owners).astype(jnp.int32) % row_count
    slot_of = jnp.zeros((row_count,), jnp.int32).at[owners].set(jnp.arange(row_count, dtype=jnp.int32))
    return data, slot_of


def gather_col(value):
    count = lax.axis_size("col")
    return jnp.stack([value] + [shifted(value, "col", d) for d in range(1, count)])


def with_ints(blocks, ints):
    extra = jnp.zeros(blocks.shape[1:], blocks.dtype).at[0, : ints.shape[0]].set(ints.astype(blocks.dtype))
    return jnp.concatenate([blocks, extra[None]])


def on_device(density, block_offset, filter_offset, position):
    extent = position.shape[0]
    slots_tile = density.shape[1]
    edge = density.shape[2]
    col_count = lax.axis_size("col")
    col_id = lax.axis_index("col")
    layer_id = lax.axis_index("layer")
    image_of = jnp.zeros((extent,), jnp.int32).at[position].set(jnp.arange(extent, dtype=jnp.int32))
    base = position[layer_id]
    ks = jnp.arange(CANDIDATES, dtype=jnp.int32)
    cand = image_of[(base + ks) % extent]

    row_payload = with_ints(
        density[cand].reshape(-1, edge, edge), block_offset[cand].reshape(-1)
    )
    gathered, slot_of = gather_rows(row_payload)
    row_blocks = CANDIDATES * slots_tile
    gathered_offsets = gathered[:, row_blocks, 0, :row_blocks].astype(jnp.int32).reshape(-1, CANDIDATES, slots_tile)

    col_of_piece = (col_id - jnp.arange(col_count, dtype=jnp.int32)) % col_count
    own_ints = jnp.concatenate([block_offset[layer_id], filter_offset[layer_id]])
    col_payload = gather_col(with_ints(density[layer_id], own_ints))
    left = col_payload[:, :slots_tile].reshape(-1, edge, edge)
    all_ints = col_payload[:, slots_tile, 0, : own_ints.shape[0]].astype(jnp.int32)
    left_offsets = all_ints[:, :slots_tile].reshape(-1)
    filter_all = all_ints[:, slots_tile:].reshape(-1)
    left_w = (col_of_piece[:, None] * slots_tile + jnp.arange(slots_tile, dtype=jnp.int32)).reshape(-1)

    t_count = slots_tile
    t_all = jnp.arange(t_count, dtype=jnp.int32)
    groups = col_id * slots_tile + t_all
    filter_own = filter_offset[layer_id].reshape(t_count, -1)
    target = groups[:, None] * extent + image_of[(base + filter_own) % extent]

    def right_columns(slot_index, k_index):
        offsets = gathered_offsets[slot_index, k_index]
        physical = (position[cand[k_index]][:, None] + offsets) % extent
        return groups[None, :] * extent + image_of[physical]

    def masked_right(slot_index, k_index):
        blocks = gathered[slot_index[None, :], k_index[None, :] * slots_tile + t_all[:, None]]
        match = right_columns(slot_index, k_index).T[:, None, :] == target[:, :, None]
        return jnp.where(match[..., None, None], blocks[:, None], jnp.zeros((), blocks.dtype))

    square_slot = slot_of[left_w]
    square_right = masked_right(square_slot, left_offsets)
    square = jnp.einsum("wxy,tjwyz->tjxz", left, square_right, preferred_element_type=jnp.float32)

    square_half = square.astype(jnp.bfloat16).reshape(-1, edge, edge)
    per_col = square_half.shape[0]
    square_all = gather_col(square_half).reshape(-1, edge, edge)
    v_all = (col_of_piece[:, None] * per_col + jnp.arange(per_col, dtype=jnp.int32)).reshape(-1)
    row_groups = slot_of.shape[0]
    cube_slot = slot_of[v_all // (col_count * per_col // row_groups)]
    cube_right = masked_right(cube_slot, filter_all)
    cube = jnp.einsum("vxy,tjvyz->tjxz", square_all, cube_right, preferred_element_type=jnp.float32)

    result = 3.0 * square - 2.0 * cube
    return result.reshape(1, -1, edge, edge)


def solution(mesh):
    placed = (P("row", "col", None, None), P("row", "col"), P("row", "col"), P())
    return jax.shard_map(
        on_device,
        mesh=mesh,
        in_specs=placed,
        out_specs=P(("row", "layer"), "col", None, None),
        check_vma=False,
    )
```

```python
import jax
import jax.numpy as jnp
from jax import lax
from jax.sharding import PartitionSpec as P

CANDIDATES = 4


def shifted(value, axis, steps):
    count = lax.axis_size(axis)
    pairs = [(source, (source + steps) % count) for source in range(count)]
    return lax.ppermute(value, axis, pairs)


def partner(value, axis):
    count = lax.axis_size(axis)
    return lax.ppermute(value, axis, [(source, source ^ 1) for source in range(count)])


def gather_rows(pair):
    row_count = lax.axis_size("row")
    z_count = row_count // 2
    row_id = lax.axis_index("row")
    z_id = row_id // 2
    x_lo = row_id % 2
    mine = pair
    theirs = partner(pair, "row")
    chunk = tuple(jnp.stack([a, b]) for a, b in zip(mine, theirs))

    def groups_of(z_source):
        z_source = z_source % z_count
        return [2 * z_source + x_lo, 2 * z_source + 1 - x_lo]

    pieces = [chunk]
    owners = groups_of(z_id)
    ahead, behind = chunk, chunk
    for distance in range(1, z_count // 2):
        ahead = shifted(ahead, "row", 2)
        behind = shifted(behind, "row", -2)
        pieces += [ahead, behind]
        owners += groups_of(z_id - distance) + groups_of(z_id + distance)
    last_ahead = shifted(tuple(a[:1] for a in ahead), "row", 2)
    last_behind = shifted(tuple(b[1:] for b in behind), "row", -2)
    pieces += [last_ahead, last_behind]
    owners += groups_of(z_id - z_count // 2)[:1] + groups_of(z_id + z_count // 2)[1:]
    data = jnp.concatenate([p[0] for p in pieces])
    offsets = jnp.concatenate([p[1] for p in pieces])
    owners = jnp.stack(owners).astype(jnp.int32) % row_count
    slot_of = jnp.zeros((row_count,), jnp.int32).at[owners].set(jnp.arange(row_count, dtype=jnp.int32))
    return data, offsets, slot_of


def gather_col(value):
    count = lax.axis_size("col")
    return jnp.stack([value] + [shifted(value, "col", d) for d in range(1, count)])


def on_device(density, block_offset, filter_offset, position):
    extent = position.shape[0]
    slots_tile = density.shape[1]
    col_count = lax.axis_size("col")
    col_id = lax.axis_index("col")
    layer_id = lax.axis_index("layer")
    image_of = jnp.zeros((extent,), jnp.int32).at[position].set(jnp.arange(extent, dtype=jnp.int32))
    base = position[layer_id]
    ks = jnp.arange(CANDIDATES, dtype=jnp.int32)
    cand = image_of[(base + ks) % extent]

    gathered, gathered_offsets, slot_of = gather_rows((density[cand], block_offset[cand]))

    col_of_piece = (col_id - jnp.arange(col_count, dtype=jnp.int32)) % col_count
    left = gather_col(density[layer_id]).reshape(-1, *density.shape[2:])
    own_ints = jnp.concatenate([block_offset[layer_id], filter_offset[layer_id]])
    all_ints = gather_col(own_ints)
    left_offsets = all_ints[:, :slots_tile].reshape(-1)
    filter_all = all_ints[:, slots_tile:].reshape(-1)
    left_w = (col_of_piece[:, None] * slots_tile + jnp.arange(slots_tile, dtype=jnp.int32)).reshape(-1)

    t_count = slots_tile
    t_all = jnp.arange(t_count, dtype=jnp.int32)
    groups = col_id * slots_tile + t_all
    filter_own = filter_offset[layer_id].reshape(t_count, -1)
    target = groups[:, None] * extent + image_of[(base + filter_own) % extent]

    def right_columns(slot_index, k_index):
        offsets = gathered_offsets[slot_index, k_index]
        physical = (position[cand[k_index]][:, None] + offsets) % extent
        return groups[None, :] * extent + image_of[physical]

    def masked_right(slot_index, k_index):
        blocks = gathered[slot_index[None, :], k_index[None, :], t_all[:, None]]
        match = right_columns(slot_index, k_index).T[:, None, :] == target[:, :, None]
        return jnp.where(match[..., None, None], blocks[:, None], jnp.zeros((), blocks.dtype))

    square_slot = slot_of[left_w]
    square_right = masked_right(square_slot, left_offsets)
    square = jnp.einsum("wxy,tjwyz->tjxz", left, square_right, preferred_element_type=jnp.float32)

    square_half = square.astype(jnp.bfloat16).reshape(-1, *square.shape[2:])
    per_col = square_half.shape[0]
    square_all = gather_col(square_half).reshape(-1, *square_half.shape[1:])
    v_all = (col_of_piece[:, None] * per_col + jnp.arange(per_col, dtype=jnp.int32)).reshape(-1)
    row_groups = slot_of.shape[0]
    cube_slot = slot_of[v_all // (col_count * per_col // row_groups)]
    cube_right = masked_right(cube_slot, filter_all)
    cube = jnp.einsum("vxy,tjvyz->tjxz", square_all, cube_right, preferred_element_type=jnp.float32)

    result = 3.0 * square - 2.0 * cube
    return result.reshape(1, -1, *result.shape[2:])


def solution(mesh):
    placed = (P("row", "col", None, None), P("row", "col"), P("row", "col"), P())
    return jax.shard_map(
        on_device,
        mesh=mesh,
        in_specs=placed,
        out_specs=P(("row", "layer"), "col", None, None),
        check_vma=False,
    )
```

```python
import jax
import jax.numpy as jnp
from jax import lax
from jax.sharding import PartitionSpec as P

CANDIDATES = 4


def shifted(value, axis, steps):
    count = lax.axis_size(axis)
    pairs = [(source, (source + steps) % count) for source in range(count)]
    return lax.ppermute(value, axis, pairs)


def partner(value, axis):
    count = lax.axis_size(axis)
    return lax.ppermute(value, axis, [(source, source ^ 1) for source in range(count)])


def gather_rows(payload, ints):
    row_count = lax.axis_size("row")
    z_count = row_count // 2
    half = payload.shape[0] // 2
    row_id = lax.axis_index("row")
    z_id = row_id // 2
    x_lo = row_id % 2
    theirs = partner(payload, "row")
    theirs_ints = partner(ints, "row")
    chunk = (jnp.concatenate([payload, theirs[:half]]), jnp.stack([ints, theirs_ints]))
    whole = payload.shape[0]

    mine_parts, front_parts, back_parts, ints_parts = [payload], [theirs[:half]], [theirs[half:]], [chunk[1]]
    z_sources = [z_id]
    ahead, behind = chunk, chunk
    for distance in range(1, z_count // 2):
        ahead = shifted(ahead, "row", 2)
        behind = shifted(behind, "row", -2)
        forwarded = partner(jnp.stack([ahead[0][half:whole], behind[0][half:whole]]), "row")
        for received, back in ((ahead, forwarded[0]), (behind, forwarded[1])):
            mine_parts.append(received[0][:whole])
            front_parts.append(received[0][whole:])
            back_parts.append(back)
            ints_parts.append(received[1])
        z_sources += [z_id - distance, z_id + distance]
    last_ahead = shifted((ahead[0][:whole], ahead[1]), "row", 2)
    last_behind = shifted(behind[0][whole:], "row", -2)
    last_back = partner(last_ahead[0][half:], "row")
    mine_parts.append(last_ahead[0])
    front_parts.append(last_behind)
    back_parts.append(last_back)
    ints_parts.append(last_ahead[1])
    z_sources.append(z_id - z_count // 2)

    mine = jnp.stack(mine_parts)
    other = jnp.concatenate([jnp.stack(front_parts), jnp.stack(back_parts)], axis=1)
    data = jnp.concatenate([mine, other])
    all_ints = jnp.stack(ints_parts)
    offsets = jnp.concatenate([all_ints[:, 0], all_ints[:, 1]])
    z_sources = jnp.stack(z_sources).astype(jnp.int32) % z_count
    owners = jnp.concatenate([2 * z_sources + x_lo, 2 * z_sources + 1 - x_lo])
    slot_of = jnp.zeros((row_count,), jnp.int32).at[owners].set(jnp.arange(row_count, dtype=jnp.int32))
    return data, offsets, slot_of


def gather_col(value):
    count = lax.axis_size("col")
    return jnp.stack([value] + [shifted(value, "col", d) for d in range(1, count)])


def on_device(density, block_offset, filter_offset, position):
    extent = position.shape[0]
    slots_tile = density.shape[1]
    col_count = lax.axis_size("col")
    col_id = lax.axis_index("col")
    layer_id = lax.axis_index("layer")
    image_of = jnp.zeros((extent,), jnp.int32).at[position].set(jnp.arange(extent, dtype=jnp.int32))
    base = position[layer_id]
    ks = jnp.arange(CANDIDATES, dtype=jnp.int32)
    cand = image_of[(base + ks) % extent]

    gathered, gathered_offsets, slot_of = gather_rows(density[cand], block_offset[cand])

    col_of_piece = (col_id - jnp.arange(col_count, dtype=jnp.int32)) % col_count
    left = gather_col(density[layer_id]).reshape(-1, *density.shape[2:])
    own_ints = jnp.concatenate([block_offset[layer_id], filter_offset[layer_id]])
    all_ints = gather_col(own_ints)
    left_offsets = all_ints[:, :slots_tile].reshape(-1)
    filter_all = all_ints[:, slots_tile:].reshape(-1)
    left_w = (col_of_piece[:, None] * slots_tile + jnp.arange(slots_tile, dtype=jnp.int32)).reshape(-1)

    t_count = slots_tile
    t_all = jnp.arange(t_count, dtype=jnp.int32)
    groups = col_id * slots_tile + t_all
    filter_own = filter_offset[layer_id].reshape(t_count, -1)
    target = groups[:, None] * extent + image_of[(base + filter_own) % extent]

    def right_columns(slot_index, k_index):
        offsets = gathered_offsets[slot_index, k_index]
        physical = (position[cand[k_index]][:, None] + offsets) % extent
        return groups[None, :] * extent + image_of[physical]

    def masked_right(slot_index, k_index):
        blocks = gathered[slot_index[None, :], k_index[None, :], t_all[:, None]]
        match = right_columns(slot_index, k_index).T[:, None, :] == target[:, :, None]
        return jnp.where(match[..., None, None], blocks[:, None], jnp.zeros((), blocks.dtype))

    square_slot = slot_of[left_w]
    square_right = masked_right(square_slot, left_offsets)
    square = jnp.einsum("wxy,tjwyz->tjxz", left, square_right, preferred_element_type=jnp.float32)

    square_half = square.astype(jnp.bfloat16).reshape(-1, *square.shape[2:])
    per_col = square_half.shape[0]
    square_all = gather_col(square_half).reshape(-1, *square_half.shape[1:])
    v_all = (col_of_piece[:, None] * per_col + jnp.arange(per_col, dtype=jnp.int32)).reshape(-1)
    row_groups = slot_of.shape[0]
    cube_slot = slot_of[v_all // (col_count * per_col // row_groups)]
    cube_right = masked_right(cube_slot, filter_all)
    cube = jnp.einsum("vxy,tjvyz->tjxz", square_all, cube_right, preferred_element_type=jnp.float32)

    result = 3.0 * square - 2.0 * cube
    return result.reshape(1, -1, *result.shape[2:])


def solution(mesh):
    placed = (P("row", "col", None, None), P("row", "col"), P("row", "col"), P())
    return jax.shard_map(
        on_device,
        mesh=mesh,
        in_specs=placed,
        out_specs=P(("row", "layer"), "col", None, None),
        check_vma=False,
    )
```

```python
import jax
import jax.numpy as jnp
from jax import lax
from jax.sharding import PartitionSpec as P

CANDIDATES = 4


def shifted(value, axis, steps):
    count = lax.axis_size(axis)
    pairs = [(source, (source + steps) % count) for source in range(count)]
    return lax.ppermute(value, axis, pairs)


def partner(value, axis):
    count = lax.axis_size(axis)
    return lax.ppermute(value, axis, [(source, source ^ 1) for source in range(count)])


def gather_rows(pair):
    row_count = lax.axis_size("row")
    z_count = row_count // 2
    row_id = lax.axis_index("row")
    z_id = row_id // 2
    x_lo = row_id % 2
    mine = pair
    theirs = partner(pair, "row")
    chunk = tuple(jnp.stack([a, b]) for a, b in zip(mine, theirs))

    def groups_of(z_source):
        z_source = z_source % z_count
        return [2 * z_source + x_lo, 2 * z_source + 1 - x_lo]

    pieces = [chunk]
    owners = groups_of(z_id)
    ahead, behind = chunk, chunk
    first_step = None
    for distance in range(1, z_count // 2):
        ahead = shifted(ahead, "row", 2)
        behind = shifted(behind, "row", -2)
        first_step = ahead
        pieces += [ahead, behind]
        owners += groups_of(z_id - distance) + groups_of(z_id + distance)
    last_ahead = shifted(tuple(a[:1] for a in ahead), "row", 2)
    last_behind = shifted(tuple(b[1:] for b in behind), "row", -2)
    pieces += [last_ahead, last_behind]
    owners += groups_of(z_id - z_count // 2)[:1] + groups_of(z_id + z_count // 2)[1:]
    data = jnp.concatenate([p[0] for p in pieces])
    offsets = jnp.concatenate([p[1] for p in pieces])
    owners = jnp.stack(owners).astype(jnp.int32) % row_count
    slot_of = jnp.zeros((row_count,), jnp.int32).at[owners].set(jnp.arange(row_count, dtype=jnp.int32))
    return data, offsets, slot_of, first_step


def gather_col(value):
    count = lax.axis_size("col")
    return jnp.stack([value] + [shifted(value, "col", d) for d in range(1, count)])


def on_device(density, block_offset, filter_offset, position):
    extent = position.shape[0]
    slots_tile = density.shape[1]
    col_count = lax.axis_size("col")
    col_id = lax.axis_index("col")
    layer_id = lax.axis_index("layer")
    image_of = jnp.zeros((extent,), jnp.int32).at[position].set(jnp.arange(extent, dtype=jnp.int32))
    base = position[layer_id]
    ks = jnp.arange(CANDIDATES, dtype=jnp.int32)
    cand = image_of[(base + ks) % extent]

    gathered, gathered_offsets, slot_of, first_step = gather_rows((density[cand], block_offset[cand]))

    col_of_piece = (col_id - jnp.arange(col_count, dtype=jnp.int32)) % col_count
    own_ints = jnp.concatenate([block_offset[layer_id], filter_offset[layer_id]])
    extra = jnp.zeros(density.shape[2:], density.dtype).at[0, : own_ints.shape[0]].set(own_ints.astype(density.dtype))
    own_payload = jnp.concatenate([density[layer_id], extra[None]])
    own_payload, _ = lax.optimization_barrier((own_payload, first_step))
    col_payload = gather_col(own_payload)
    left = col_payload[:, :slots_tile].reshape(-1, *density.shape[2:])
    all_ints = col_payload[:, slots_tile, 0, : own_ints.shape[0]].astype(jnp.int32)
    left_offsets = all_ints[:, :slots_tile].reshape(-1)
    filter_all = all_ints[:, slots_tile:].reshape(-1)
    left_w = (col_of_piece[:, None] * slots_tile + jnp.arange(slots_tile, dtype=jnp.int32)).reshape(-1)

    t_count = slots_tile
    t_all = jnp.arange(t_count, dtype=jnp.int32)
    groups = col_id * slots_tile + t_all
    filter_own = filter_offset[layer_id].reshape(t_count, -1)
    target = groups[:, None] * extent + image_of[(base + filter_own) % extent]

    def right_columns(slot_index, k_index):
        offsets = gathered_offsets[slot_index, k_index]
        physical = (position[cand[k_index]][:, None] + offsets) % extent
        return groups[None, :] * extent + image_of[physical]

    def masked_right(slot_index, k_index):
        blocks = gathered[slot_index[None, :], k_index[None, :], t_all[:, None]]
        match = right_columns(slot_index, k_index).T[:, None, :] == target[:, :, None]
        return jnp.where(match[..., None, None], blocks[:, None], jnp.zeros((), blocks.dtype))

    square_slot = slot_of[left_w]
    square_right = masked_right(square_slot, left_offsets)
    square = jnp.einsum("wxy,tjwyz->tjxz", left, square_right, preferred_element_type=jnp.float32)

    square_half = square.astype(jnp.bfloat16).reshape(-1, *square.shape[2:])
    per_col = square_half.shape[0]
    square_all = gather_col(square_half).reshape(-1, *square_half.shape[1:])
    v_all = (col_of_piece[:, None] * per_col + jnp.arange(per_col, dtype=jnp.int32)).reshape(-1)
    row_groups = slot_of.shape[0]
    cube_slot = slot_of[v_all // (col_count * per_col // row_groups)]
    cube_right = masked_right(cube_slot, filter_all)
    cube = jnp.einsum("vxy,tjvyz->tjxz", square_all, cube_right, preferred_element_type=jnp.float32)

    result = 3.0 * square - 2.0 * cube
    return result.reshape(1, -1, *result.shape[2:])


def solution(mesh):
    placed = (P("row", "col", None, None), P("row", "col"), P("row", "col"), P())
    return jax.shard_map(
        on_device,
        mesh=mesh,
        in_specs=placed,
        out_specs=P(("row", "layer"), "col", None, None),
        check_vma=False,
    )
```

```python
import jax
import jax.numpy as jnp
from jax import lax
from jax.sharding import PartitionSpec as P

CANDIDATES = 4


def shifted(value, axis, steps):
    count = lax.axis_size(axis)
    pairs = [(source, (source + steps) % count) for source in range(count)]
    return lax.ppermute(value, axis, pairs)


def partner(value, axis):
    count = lax.axis_size(axis)
    return lax.ppermute(value, axis, [(source, source ^ 1) for source in range(count)])


def gather_rows(payload):
    row_count = lax.axis_size("row")
    z_count = row_count // 2
    row_id = lax.axis_index("row")
    z_id = row_id // 2
    x_lo = row_id % 2
    chunk = jnp.stack([payload, partner(payload, "row")])

    def groups_of(z_source):
        z_source = z_source % z_count
        return [2 * z_source + x_lo, 2 * z_source + 1 - x_lo]

    pieces = [chunk]
    owners = groups_of(z_id)
    ahead, behind = chunk, chunk
    for distance in range(1, z_count // 2):
        ahead = shifted(ahead, "row", 2)
        behind = shifted(behind, "row", -2)
        pieces += [ahead, behind]
        owners += groups_of(z_id - distance) + groups_of(z_id + distance)
    third_step = ahead
    pieces += [shifted(ahead[:1], "row", 2), shifted(behind[1:], "row", -2)]
    owners += groups_of(z_id - z_count // 2)[:1] + groups_of(z_id + z_count // 2)[1:]
    owners = jnp.stack(owners).astype(jnp.int32) % row_count
    slot_of = jnp.zeros((row_count,), jnp.int32).at[owners].set(jnp.arange(row_count, dtype=jnp.int32))
    return pieces, slot_of, third_step


def gather_col(value):
    count = lax.axis_size("col")
    return jnp.stack([value] + [shifted(value, "col", d) for d in range(1, count)])


def on_device(density, block_offset, filter_offset, position):
    extent = position.shape[0]
    slots_tile = density.shape[1]
    col_count = lax.axis_size("col")
    col_id = lax.axis_index("col")
    layer_id = lax.axis_index("layer")
    image_of = jnp.zeros((extent,), jnp.int32).at[position].set(jnp.arange(extent, dtype=jnp.int32))
    base = position[layer_id]
    ks = jnp.arange(CANDIDATES, dtype=jnp.int32)
    cand = image_of[(base + ks) % extent]

    edge = density.shape[2]
    row_blocks = CANDIDATES * slots_tile
    row_extra = jnp.zeros((edge, edge), density.dtype).at[0, :row_blocks].set(
        block_offset[cand].reshape(-1).astype(density.dtype)
    )
    row_payload = jnp.concatenate([density[cand].reshape(-1, edge, edge), row_extra[None]])
    pieces, slot_of, first_step = gather_rows(row_payload)
    gathered = jnp.concatenate([p[:, :row_blocks] for p in pieces]).reshape(-1, CANDIDATES, slots_tile, edge, edge)
    gathered_offsets = (
        jnp.concatenate([p[:, row_blocks, 0, :row_blocks] for p in pieces])
        .astype(jnp.int32)
        .reshape(-1, CANDIDATES, slots_tile)
    )

    col_of_piece = (col_id - jnp.arange(col_count, dtype=jnp.int32)) % col_count
    own_ints = jnp.concatenate([block_offset[layer_id], filter_offset[layer_id]])
    extra = jnp.zeros(density.shape[2:], density.dtype).at[0, : own_ints.shape[0]].set(own_ints.astype(density.dtype))
    own_payload = jnp.concatenate([density[layer_id], extra[None]])
    own_payload, _ = lax.optimization_barrier((own_payload, first_step))
    col_payload = gather_col(own_payload)
    left = col_payload[:, :slots_tile].reshape(-1, *density.shape[2:])
    all_ints = col_payload[:, slots_tile, 0, : own_ints.shape[0]].astype(jnp.int32)
    left_offsets = all_ints[:, :slots_tile].reshape(-1)
    filter_all = all_ints[:, slots_tile:].reshape(-1)
    left_w = (col_of_piece[:, None] * slots_tile + jnp.arange(slots_tile, dtype=jnp.int32)).reshape(-1)

    t_count = slots_tile
    t_all = jnp.arange(t_count, dtype=jnp.int32)
    groups = col_id * slots_tile + t_all
    filter_own = filter_offset[layer_id].reshape(t_count, -1)
    target = groups[:, None] * extent + image_of[(base + filter_own) % extent]

    def right_columns(slot_index, k_index):
        offsets = gathered_offsets[slot_index, k_index]
        physical = (position[cand[k_index]][:, None] + offsets) % extent
        return groups[None, :] * extent + image_of[physical]

    def masked_right(slot_index, k_index):
        blocks = gathered[slot_index[None, :], k_index[None, :], t_all[:, None]]
        match = right_columns(slot_index, k_index).T[:, None, :] == target[:, :, None]
        return jnp.where(match[..., None, None], blocks[:, None], jnp.zeros((), blocks.dtype))

    square_slot = slot_of[left_w]
    square_right = masked_right(square_slot, left_offsets)
    square = jnp.einsum("wxy,tjwyz->tjxz", left, square_right, preferred_element_type=jnp.float32)

    square_half = square.astype(jnp.bfloat16).reshape(-1, *square.shape[2:])
    per_col = square_half.shape[0]
    square_all = gather_col(square_half).reshape(-1, *square_half.shape[1:])
    v_all = (col_of_piece[:, None] * per_col + jnp.arange(per_col, dtype=jnp.int32)).reshape(-1)
    row_groups = slot_of.shape[0]
    cube_slot = slot_of[v_all // (col_count * per_col // row_groups)]
    cube_right = masked_right(cube_slot, filter_all)
    cube = jnp.einsum("vxy,tjvyz->tjxz", square_all, cube_right, preferred_element_type=jnp.float32)

    result = 3.0 * square - 2.0 * cube
    return result.reshape(1, -1, *result.shape[2:])


def solution(mesh):
    placed = (P("row", "col", None, None), P("row", "col"), P("row", "col"), P())
    return jax.shard_map(
        on_device,
        mesh=mesh,
        in_specs=placed,
        out_specs=P(("row", "layer"), "col", None, None),
        check_vma=False,
    )
```

```python
import jax
import jax.numpy as jnp
from jax import lax
from jax.sharding import PartitionSpec as P

CANDIDATES = 4


def shifted(value, axis, steps):
    count = lax.axis_size(axis)
    pairs = [(source, (source + steps) % count) for source in range(count)]
    return lax.ppermute(value, axis, pairs)


def partner(value, axis):
    count = lax.axis_size(axis)
    return lax.ppermute(value, axis, [(source, source ^ 1) for source in range(count)])


def gather_rows(pair):
    row_count = lax.axis_size("row")
    z_count = row_count // 2
    row_id = lax.axis_index("row")
    z_id = row_id // 2
    x_lo = row_id % 2
    mine = pair
    theirs = partner(pair, "row")
    chunk = tuple(jnp.stack([a, b]) for a, b in zip(mine, theirs))

    def groups_of(z_source):
        z_source = z_source % z_count
        return [2 * z_source + x_lo, 2 * z_source + 1 - x_lo]

    pieces = [chunk]
    owners = groups_of(z_id)
    ahead, behind = chunk, chunk
    first_step = None
    for distance in range(1, z_count // 2):
        ahead = shifted(ahead, "row", 2)
        behind = shifted(behind, "row", -2)
        first_step = ahead
        pieces += [ahead, behind]
        owners += groups_of(z_id - distance) + groups_of(z_id + distance)
    last_ahead = shifted(tuple(a[:1] for a in ahead), "row", 2)
    last_behind = shifted(tuple(b[1:] for b in behind), "row", -2)
    pieces += [last_ahead, last_behind]
    owners += groups_of(z_id - z_count // 2)[:1] + groups_of(z_id + z_count // 2)[1:]
    data = jnp.concatenate([p[0] for p in pieces])
    offsets = jnp.concatenate([p[1] for p in pieces])
    owners = jnp.stack(owners).astype(jnp.int32) % row_count
    slot_of = jnp.zeros((row_count,), jnp.int32).at[owners].set(jnp.arange(row_count, dtype=jnp.int32))
    return data, offsets, slot_of, last_ahead[0]


def gather_col(value):
    count = lax.axis_size("col")
    return jnp.stack([value] + [shifted(value, "col", d) for d in range(1, count)])


def on_device(density, block_offset, filter_offset, position):
    extent = position.shape[0]
    slots_tile = density.shape[1]
    col_count = lax.axis_size("col")
    col_id = lax.axis_index("col")
    layer_id = lax.axis_index("layer")
    image_of = jnp.zeros((extent,), jnp.int32).at[position].set(jnp.arange(extent, dtype=jnp.int32))
    base = position[layer_id]
    ks = jnp.arange(CANDIDATES, dtype=jnp.int32)
    cand = image_of[(base + ks) % extent]

    gathered, gathered_offsets, slot_of, first_step = gather_rows((density[cand], block_offset[cand]))

    col_of_piece = (col_id - jnp.arange(col_count, dtype=jnp.int32)) % col_count
    own_ints = jnp.concatenate([block_offset[layer_id], filter_offset[layer_id]])
    extra = jnp.zeros(density.shape[2:], density.dtype).at[0, : own_ints.shape[0]].set(own_ints.astype(density.dtype))
    own_payload = jnp.concatenate([density[layer_id], extra[None]])
    own_payload, _ = lax.optimization_barrier((own_payload, first_step))
    col_payload = gather_col(own_payload)
    left = col_payload[:, :slots_tile].reshape(-1, *density.shape[2:])
    all_ints = col_payload[:, slots_tile, 0, : own_ints.shape[0]].astype(jnp.int32)
    left_offsets = all_ints[:, :slots_tile].reshape(-1)
    filter_all = all_ints[:, slots_tile:].reshape(-1)
    left_w = (col_of_piece[:, None] * slots_tile + jnp.arange(slots_tile, dtype=jnp.int32)).reshape(-1)

    t_count = slots_tile
    t_all = jnp.arange(t_count, dtype=jnp.int32)
    groups = col_id * slots_tile + t_all
    filter_own = filter_offset[layer_id].reshape(t_count, -1)
    target = groups[:, None] * extent + image_of[(base + filter_own) % extent]

    def right_columns(slot_index, k_index):
        offsets = gathered_offsets[slot_index, k_index]
        physical = (position[cand[k_index]][:, None] + offsets) % extent
        return groups[None, :] * extent + image_of[physical]

    def masked_right(slot_index, k_index):
        blocks = gathered[slot_index[None, :], k_index[None, :], t_all[:, None]]
        match = right_columns(slot_index, k_index).T[:, None, :] == target[:, :, None]
        return jnp.where(match[..., None, None], blocks[:, None], jnp.zeros((), blocks.dtype))

    square_slot = slot_of[left_w]
    square_right = masked_right(square_slot, left_offsets)
    square = jnp.einsum("wxy,tjwyz->tjxz", left, square_right, preferred_element_type=jnp.float32)

    square_half = square.astype(jnp.bfloat16).reshape(-1, *square.shape[2:])
    per_col = square_half.shape[0]
    square_all = gather_col(square_half).reshape(-1, *square_half.shape[1:])
    v_all = (col_of_piece[:, None] * per_col + jnp.arange(per_col, dtype=jnp.int32)).reshape(-1)
    row_groups = slot_of.shape[0]
    cube_slot = slot_of[v_all // (col_count * per_col // row_groups)]
    cube_right = masked_right(cube_slot, filter_all)
    cube = jnp.einsum("vxy,tjvyz->tjxz", square_all, cube_right, preferred_element_type=jnp.float32)

    result = 3.0 * square - 2.0 * cube
    return result.reshape(1, -1, *result.shape[2:])


def solution(mesh):
    placed = (P("row", "col", None, None), P("row", "col"), P("row", "col"), P())
    return jax.shard_map(
        on_device,
        mesh=mesh,
        in_specs=placed,
        out_specs=P(("row", "layer"), "col", None, None),
        check_vma=False,
    )
```

```python
import jax
import jax.numpy as jnp
from jax import lax
from jax.sharding import PartitionSpec as P

CANDIDATES = 4


def shifted(value, axis, steps):
    count = lax.axis_size(axis)
    pairs = [(source, (source + steps) % count) for source in range(count)]
    return lax.ppermute(value, axis, pairs)


def partner(value, axis):
    count = lax.axis_size(axis)
    return lax.ppermute(value, axis, [(source, source ^ 1) for source in range(count)])


def gather_rows(pair):
    row_count = lax.axis_size("row")
    z_count = row_count // 2
    row_id = lax.axis_index("row")
    z_id = row_id // 2
    x_lo = row_id % 2
    mine = pair
    theirs = partner(pair, "row")
    chunk = tuple(jnp.stack([a, b]) for a, b in zip(mine, theirs))

    def groups_of(z_source):
        z_source = z_source % z_count
        return [2 * z_source + x_lo, 2 * z_source + 1 - x_lo]

    pieces = [chunk]
    owners = groups_of(z_id)
    ahead, behind = chunk, chunk
    first_step = None
    for distance in range(1, z_count // 2):
        ahead = shifted(ahead, "row", 2)
        behind = shifted(behind, "row", -2)
        first_step = ahead
        pieces += [ahead, behind]
        owners += groups_of(z_id - distance) + groups_of(z_id + distance)
    last_ahead = shifted(tuple(a[:1] for a in ahead), "row", 2)
    last_behind = shifted(tuple(b[1:] for b in behind), "row", -2)
    pieces += [last_ahead, last_behind]
    owners += groups_of(z_id - z_count // 2)[:1] + groups_of(z_id + z_count // 2)[1:]
    joined = tuple(jnp.concatenate([p[i] for p in pieces]) for i in range(len(chunk)))
    owners = jnp.stack(owners).astype(jnp.int32) % row_count
    slot_of = jnp.zeros((row_count,), jnp.int32).at[owners].set(jnp.arange(row_count, dtype=jnp.int32))
    return joined, slot_of, first_step


def gather_col(value):
    count = lax.axis_size("col")
    return jnp.stack([value] + [shifted(value, "col", d) for d in range(1, count)])


def on_device(density, block_offset, filter_offset, position):
    extent = position.shape[0]
    slots_tile = density.shape[1]
    col_count = lax.axis_size("col")
    col_id = lax.axis_index("col")
    layer_id = lax.axis_index("layer")
    image_of = jnp.zeros((extent,), jnp.int32).at[position].set(jnp.arange(extent, dtype=jnp.int32))
    base = position[layer_id]
    ks = jnp.arange(CANDIDATES, dtype=jnp.int32)
    cand = image_of[(base + ks) % extent]

    split = CANDIDATES // 2
    (near, gathered_offsets), slot_of, first_step = gather_rows((density[cand[:split]], block_offset[cand]))
    later_payload, _ = lax.optimization_barrier((density[cand[split:]], near))
    (far,), _, _ = gather_rows((later_payload,))

    col_of_piece = (col_id - jnp.arange(col_count, dtype=jnp.int32)) % col_count
    own_ints = jnp.concatenate([block_offset[layer_id], filter_offset[layer_id]])
    extra = jnp.zeros(density.shape[2:], density.dtype).at[0, : own_ints.shape[0]].set(own_ints.astype(density.dtype))
    own_payload = jnp.concatenate([density[layer_id], extra[None]])
    own_payload, _ = lax.optimization_barrier((own_payload, first_step))
    col_payload = gather_col(own_payload)
    left = col_payload[:, :slots_tile].reshape(-1, *density.shape[2:])
    all_ints = col_payload[:, slots_tile, 0, : own_ints.shape[0]].astype(jnp.int32)
    left_offsets = all_ints[:, :slots_tile].reshape(-1)
    filter_all = all_ints[:, slots_tile:].reshape(-1)
    left_w = (col_of_piece[:, None] * slots_tile + jnp.arange(slots_tile, dtype=jnp.int32)).reshape(-1)

    t_count = slots_tile
    t_all = jnp.arange(t_count, dtype=jnp.int32)
    groups = col_id * slots_tile + t_all
    filter_own = filter_offset[layer_id].reshape(t_count, -1)
    target = groups[:, None] * extent + image_of[(base + filter_own) % extent]

    def right_columns(slot_index, k_index):
        offsets = gathered_offsets[slot_index, k_index]
        physical = (position[cand[k_index]][:, None] + offsets) % extent
        return groups[None, :] * extent + image_of[physical]

    def masked_right(slot_index, k_index, far_too):
        slots, ks_ = slot_index[None, :], k_index[None, :]
        blocks = near[slots, jnp.minimum(ks_, split - 1), t_all[:, None]]
        if far_too:
            blocks = jnp.where(
                (ks_ >= split)[..., None, None], far[slots, jnp.maximum(ks_ - split, 0), t_all[:, None]], blocks
            )
        match = right_columns(slot_index, k_index).T[:, None, :] == target[:, :, None]
        return jnp.where(match[..., None, None], blocks[:, None], jnp.zeros((), blocks.dtype))

    square_slot = slot_of[left_w]
    square_right = masked_right(square_slot, left_offsets, False)
    square = jnp.einsum("wxy,tjwyz->tjxz", left, square_right, preferred_element_type=jnp.float32)

    square_half = square.astype(jnp.bfloat16).reshape(-1, *square.shape[2:])
    per_col = square_half.shape[0]
    square_all = gather_col(square_half).reshape(-1, *square_half.shape[1:])
    v_all = (col_of_piece[:, None] * per_col + jnp.arange(per_col, dtype=jnp.int32)).reshape(-1)
    row_groups = slot_of.shape[0]
    cube_slot = slot_of[v_all // (col_count * per_col // row_groups)]
    cube_right = masked_right(cube_slot, filter_all, True)
    cube = jnp.einsum("vxy,tjvyz->tjxz", square_all, cube_right, preferred_element_type=jnp.float32)

    result = 3.0 * square - 2.0 * cube
    return result.reshape(1, -1, *result.shape[2:])


def solution(mesh):
    placed = (P("row", "col", None, None), P("row", "col"), P("row", "col"), P())
    return jax.shard_map(
        on_device,
        mesh=mesh,
        in_specs=placed,
        out_specs=P(("row", "layer"), "col", None, None),
        check_vma=False,
    )
```

```python
import jax
import jax.numpy as jnp
from jax import lax
from jax.experimental import pallas as pl
from jax.sharding import PartitionSpec as P

CANDIDATES = 4


def shifted(value, axis, steps):
    count = lax.axis_size(axis)
    pairs = [(source, (source + steps) % count) for source in range(count)]
    return lax.ppermute(value, axis, pairs)


def partner(value, axis):
    count = lax.axis_size(axis)
    return lax.ppermute(value, axis, [(source, source ^ 1) for source in range(count)])


def gather_rows(pair):
    row_count = lax.axis_size("row")
    z_count = row_count // 2
    row_id = lax.axis_index("row")
    z_id = row_id // 2
    x_lo = row_id % 2
    mine = pair
    theirs = partner(pair, "row")
    chunk = tuple(jnp.stack([a, b]) for a, b in zip(mine, theirs))

    def groups_of(z_source):
        z_source = z_source % z_count
        return [2 * z_source + x_lo, 2 * z_source + 1 - x_lo]

    pieces = [chunk]
    owners = groups_of(z_id)
    ahead, behind = chunk, chunk
    first_step = None
    for distance in range(1, z_count // 2):
        ahead = shifted(ahead, "row", 2)
        behind = shifted(behind, "row", -2)
        first_step = ahead
        pieces += [ahead, behind]
        owners += groups_of(z_id - distance) + groups_of(z_id + distance)
    last_ahead = shifted(tuple(a[:1] for a in ahead), "row", 2)
    last_behind = shifted(tuple(b[1:] for b in behind), "row", -2)
    pieces += [last_ahead, last_behind]
    owners += groups_of(z_id - z_count // 2)[:1] + groups_of(z_id + z_count // 2)[1:]
    data = jnp.concatenate([p[0] for p in pieces])
    offsets = jnp.concatenate([p[1] for p in pieces])
    owners = jnp.stack(owners).astype(jnp.int32) % row_count
    slot_of = jnp.zeros((row_count,), jnp.int32).at[owners].set(jnp.arange(row_count, dtype=jnp.int32))
    return data, offsets, slot_of, first_step


def gather_col(value):
    count = lax.axis_size("col")
    return jnp.stack([value] + [shifted(value, "col", d) for d in range(1, count)])


def transpose_blocks(blocks):
    count, edge = blocks.shape[0], blocks.shape[1]

    def kernel(x_ref, o_ref):
        o_ref[0] = x_ref[0].astype(jnp.float32).T.astype(o_ref.dtype)

    spec = pl.BlockSpec((1, edge, edge), lambda i: (i, 0, 0))
    return pl.pallas_call(
        kernel,
        out_shape=jax.ShapeDtypeStruct(blocks.shape, blocks.dtype),
        grid=(count,),
        in_specs=[spec],
        out_specs=spec,
        cost_estimate=pl.CostEstimate(flops=0, bytes_accessed=2 * blocks.size * 2, transcendentals=0),
    )(blocks)


def on_device(density, block_offset, filter_offset, position):
    extent = position.shape[0]
    slots_tile = density.shape[1]
    col_count = lax.axis_size("col")
    col_id = lax.axis_index("col")
    layer_id = lax.axis_index("layer")
    image_of = jnp.zeros((extent,), jnp.int32).at[position].set(jnp.arange(extent, dtype=jnp.int32))
    base = position[layer_id]
    ks = jnp.arange(CANDIDATES, dtype=jnp.int32)
    cand = image_of[(base + ks) % extent]

    picked = density[cand]
    right_payload = transpose_blocks(picked.reshape(-1, *picked.shape[2:])).reshape(picked.shape)
    gathered, gathered_offsets, slot_of, first_step = gather_rows((right_payload, block_offset[cand]))

    col_of_piece = (col_id - jnp.arange(col_count, dtype=jnp.int32)) % col_count
    own_ints = jnp.concatenate([block_offset[layer_id], filter_offset[layer_id]])
    extra = jnp.zeros(density.shape[2:], density.dtype).at[0, : own_ints.shape[0]].set(own_ints.astype(density.dtype))
    own_payload = jnp.concatenate([density[layer_id], extra[None]])
    own_payload, _ = lax.optimization_barrier((own_payload, first_step))
    col_payload = gather_col(own_payload)
    left = col_payload[:, :slots_tile].reshape(-1, *density.shape[2:])
    all_ints = col_payload[:, slots_tile, 0, : own_ints.shape[0]].astype(jnp.int32)
    left_offsets = all_ints[:, :slots_tile].reshape(-1)
    filter_all = all_ints[:, slots_tile:].reshape(-1)
    left_w = (col_of_piece[:, None] * slots_tile + jnp.arange(slots_tile, dtype=jnp.int32)).reshape(-1)

    t_count = slots_tile
    t_all = jnp.arange(t_count, dtype=jnp.int32)
    groups = col_id * slots_tile + t_all
    filter_own = filter_offset[layer_id].reshape(t_count, -1)
    target = groups[:, None] * extent + image_of[(base + filter_own) % extent]

    def right_columns(slot_index, k_index):
        offsets = gathered_offsets[slot_index, k_index]
        physical = (position[cand[k_index]][:, None] + offsets) % extent
        return groups[None, :] * extent + image_of[physical]

    def masked_right(slot_index, k_index):
        blocks = gathered[slot_index[None, :], k_index[None, :], t_all[:, None]]
        match = right_columns(slot_index, k_index).T[:, None, :] == target[:, :, None]
        return jnp.where(match[..., None, None], blocks[:, None], jnp.zeros((), blocks.dtype))

    square_slot = slot_of[left_w]
    square_right = masked_right(square_slot, left_offsets)
    square = jnp.einsum("wxy,tjwzy->tjxz", left, square_right, preferred_element_type=jnp.float32)

    square_half = square.astype(jnp.bfloat16).reshape(-1, *square.shape[2:])
    per_col = square_half.shape[0]
    square_all = gather_col(square_half).reshape(-1, *square_half.shape[1:])
    v_all = (col_of_piece[:, None] * per_col + jnp.arange(per_col, dtype=jnp.int32)).reshape(-1)
    row_groups = slot_of.shape[0]
    cube_slot = slot_of[v_all // (col_count * per_col // row_groups)]
    cube_right = masked_right(cube_slot, filter_all)
    cube = jnp.einsum("vxy,tjvzy->tjxz", square_all, cube_right, preferred_element_type=jnp.float32)

    result = 3.0 * square - 2.0 * cube
    return result.reshape(1, -1, *result.shape[2:])


def solution(mesh):
    placed = (P("row", "col", None, None), P("row", "col"), P("row", "col"), P())
    return jax.shard_map(
        on_device,
        mesh=mesh,
        in_specs=placed,
        out_specs=P(("row", "layer"), "col", None, None),
        check_vma=False,
    )
```

```python
import jax
import jax.numpy as jnp
from jax import lax
from jax.experimental import pallas as pl
from jax.sharding import PartitionSpec as P

CANDIDATES = 4


def shifted(value, axis, steps):
    count = lax.axis_size(axis)
    pairs = [(source, (source + steps) % count) for source in range(count)]
    return lax.ppermute(value, axis, pairs)


def partner(value, axis):
    count = lax.axis_size(axis)
    return lax.ppermute(value, axis, [(source, source ^ 1) for source in range(count)])


def gather_rows(pair):
    row_count = lax.axis_size("row")
    z_count = row_count // 2
    row_id = lax.axis_index("row")
    z_id = row_id // 2
    x_lo = row_id % 2
    mine = pair
    theirs = partner(pair, "row")
    chunk = tuple(jnp.stack([a, b]) for a, b in zip(mine, theirs))

    def groups_of(z_source):
        z_source = z_source % z_count
        return [2 * z_source + x_lo, 2 * z_source + 1 - x_lo]

    pieces = [chunk]
    owners = groups_of(z_id)
    ahead, behind = chunk, chunk
    first_step = None
    for distance in range(1, z_count // 2):
        ahead = shifted(ahead, "row", 2)
        behind = shifted(behind, "row", -2)
        first_step = ahead
        pieces += [ahead, behind]
        owners += groups_of(z_id - distance) + groups_of(z_id + distance)
    last_ahead = shifted(tuple(a[:1] for a in ahead), "row", 2)
    last_behind = shifted(tuple(b[1:] for b in behind), "row", -2)
    pieces += [last_ahead, last_behind]
    owners += groups_of(z_id - z_count // 2)[:1] + groups_of(z_id + z_count // 2)[1:]
    data = jnp.concatenate([p[0] for p in pieces])
    offsets = jnp.concatenate([p[1] for p in pieces])
    owners = jnp.stack(owners).astype(jnp.int32) % row_count
    slot_of = jnp.zeros((row_count,), jnp.int32).at[owners].set(jnp.arange(row_count, dtype=jnp.int32))
    return data, offsets, slot_of, first_step


def gather_col(value):
    count = lax.axis_size("col")
    return jnp.stack([value] + [shifted(value, "col", d) for d in range(1, count)])


def transpose_blocks(blocks):
    count = blocks.shape[0]

    def kernel(x_ref, o_ref):
        for index in range(count):
            o_ref[index] = x_ref[index].astype(jnp.float32).T.astype(o_ref.dtype)

    spec = pl.BlockSpec(blocks.shape, lambda i: (0, 0, 0))
    return pl.pallas_call(
        kernel,
        out_shape=jax.ShapeDtypeStruct(blocks.shape, blocks.dtype),
        grid=(1,),
        in_specs=[spec],
        out_specs=spec,
        cost_estimate=pl.CostEstimate(flops=0, bytes_accessed=2 * blocks.size * 2, transcendentals=0),
    )(blocks)


def on_device(density, block_offset, filter_offset, position):
    extent = position.shape[0]
    slots_tile = density.shape[1]
    col_count = lax.axis_size("col")
    col_id = lax.axis_index("col")
    layer_id = lax.axis_index("layer")
    image_of = jnp.zeros((extent,), jnp.int32).at[position].set(jnp.arange(extent, dtype=jnp.int32))
    base = position[layer_id]
    ks = jnp.arange(CANDIDATES, dtype=jnp.int32)
    cand = image_of[(base + ks) % extent]

    picked = density[cand]
    right_payload = transpose_blocks(picked.reshape(-1, *picked.shape[2:])).reshape(picked.shape)
    gathered, gathered_offsets, slot_of, first_step = gather_rows((right_payload, block_offset[cand]))

    col_of_piece = (col_id - jnp.arange(col_count, dtype=jnp.int32)) % col_count
    own_ints = jnp.concatenate([block_offset[layer_id], filter_offset[layer_id]])
    extra = jnp.zeros(density.shape[2:], density.dtype).at[0, : own_ints.shape[0]].set(own_ints.astype(density.dtype))
    own_payload = jnp.concatenate([density[layer_id], extra[None]])
    own_payload, _ = lax.optimization_barrier((own_payload, first_step))
    col_payload = gather_col(own_payload)
    left = col_payload[:, :slots_tile].reshape(-1, *density.shape[2:])
    all_ints = col_payload[:, slots_tile, 0, : own_ints.shape[0]].astype(jnp.int32)
    left_offsets = all_ints[:, :slots_tile].reshape(-1)
    filter_all = all_ints[:, slots_tile:].reshape(-1)
    left_w = (col_of_piece[:, None] * slots_tile + jnp.arange(slots_tile, dtype=jnp.int32)).reshape(-1)

    t_count = slots_tile
    t_all = jnp.arange(t_count, dtype=jnp.int32)
    groups = col_id * slots_tile + t_all
    filter_own = filter_offset[layer_id].reshape(t_count, -1)
    target = groups[:, None] * extent + image_of[(base + filter_own) % extent]

    def right_columns(slot_index, k_index):
        offsets = gathered_offsets[slot_index, k_index]
        physical = (position[cand[k_index]][:, None] + offsets) % extent
        return groups[None, :] * extent + image_of[physical]

    def masked_right(slot_index, k_index):
        blocks = gathered[slot_index[None, :], k_index[None, :], t_all[:, None]]
        match = right_columns(slot_index, k_index).T[:, None, :] == target[:, :, None]
        return jnp.where(match[..., None, None], blocks[:, None], jnp.zeros((), blocks.dtype))

    square_slot = slot_of[left_w]
    square_right = masked_right(square_slot, left_offsets)
    square = jnp.einsum("wxy,tjwzy->tjxz", left, square_right, preferred_element_type=jnp.float32)

    square_half = square.astype(jnp.bfloat16).reshape(-1, *square.shape[2:])
    per_col = square_half.shape[0]
    square_all = gather_col(square_half).reshape(-1, *square_half.shape[1:])
    v_all = (col_of_piece[:, None] * per_col + jnp.arange(per_col, dtype=jnp.int32)).reshape(-1)
    row_groups = slot_of.shape[0]
    cube_slot = slot_of[v_all // (col_count * per_col // row_groups)]
    cube_right = masked_right(cube_slot, filter_all)
    cube = jnp.einsum("vxy,tjvzy->tjxz", square_all, cube_right, preferred_element_type=jnp.float32)

    result = 3.0 * square - 2.0 * cube
    return result.reshape(1, -1, *result.shape[2:])


def solution(mesh):
    placed = (P("row", "col", None, None), P("row", "col"), P("row", "col"), P())
    return jax.shard_map(
        on_device,
        mesh=mesh,
        in_specs=placed,
        out_specs=P(("row", "layer"), "col", None, None),
        check_vma=False,
    )
```

```python
import jax
import jax.numpy as jnp
from jax import lax
from jax.experimental import pallas as pl
from jax.experimental.pallas import tpu as pltpu
from jax.sharding import PartitionSpec as P

CANDIDATES = 4


def shifted(value, axis, steps):
    count = lax.axis_size(axis)
    pairs = [(source, (source + steps) % count) for source in range(count)]
    return lax.ppermute(value, axis, pairs)


def partner(value, axis):
    count = lax.axis_size(axis)
    return lax.ppermute(value, axis, [(source, source ^ 1) for source in range(count)])


def gather_rows(pair):
    row_count = lax.axis_size("row")
    z_count = row_count // 2
    row_id = lax.axis_index("row")
    z_id = row_id // 2
    x_lo = row_id % 2
    mine = pair
    theirs = partner(pair, "row")
    chunk = tuple(jnp.stack([a, b]) for a, b in zip(mine, theirs))

    def groups_of(z_source):
        z_source = z_source % z_count
        return [2 * z_source + x_lo, 2 * z_source + 1 - x_lo]

    pieces = [chunk]
    owners = groups_of(z_id)
    ahead, behind = chunk, chunk
    first_step = None
    for distance in range(1, z_count // 2):
        ahead = shifted(ahead, "row", 2)
        behind = shifted(behind, "row", -2)
        first_step = ahead
        pieces += [ahead, behind]
        owners += groups_of(z_id - distance) + groups_of(z_id + distance)
    last_ahead = shifted(tuple(a[:1] for a in ahead), "row", 2)
    last_behind = shifted(tuple(b[1:] for b in behind), "row", -2)
    pieces += [last_ahead, last_behind]
    owners += groups_of(z_id - z_count // 2)[:1] + groups_of(z_id + z_count // 2)[1:]
    data = jnp.concatenate([p[0] for p in pieces])
    offsets = jnp.concatenate([p[1] for p in pieces])
    owners = jnp.stack(owners).astype(jnp.int32) % row_count
    slot_of = jnp.zeros((row_count,), jnp.int32).at[owners].set(jnp.arange(row_count, dtype=jnp.int32))
    return data, offsets, slot_of, first_step


def gather_col(value):
    count = lax.axis_size("col")
    return jnp.stack([value] + [shifted(value, "col", d) for d in range(1, count)])


def picked_transposed(density, rows):
    slots, edge = density.shape[1], density.shape[2]

    def kernel(rows_ref, x_ref, o_ref):
        for slot in range(slots):
            o_ref[0, slot] = x_ref[0, slot].astype(jnp.float32).T.astype(o_ref.dtype)

    block = (1, slots, edge, edge)
    grid_spec = pltpu.PrefetchScalarGridSpec(
        num_scalar_prefetch=1,
        grid=(rows.shape[0],),
        in_specs=[pl.BlockSpec(block, lambda i, rows_ref: (rows_ref[i], 0, 0, 0))],
        out_specs=pl.BlockSpec(block, lambda i, rows_ref: (i, 0, 0, 0)),
    )
    out_shape = jax.ShapeDtypeStruct((rows.shape[0],) + density.shape[1:], density.dtype)
    return pl.pallas_call(
        kernel,
        out_shape=out_shape,
        grid_spec=grid_spec,
        cost_estimate=pl.CostEstimate(flops=0, bytes_accessed=2 * 2 * rows.shape[0] * slots * edge * edge, transcendentals=0),
    )(rows, density)


def on_device(density, block_offset, filter_offset, position):
    extent = position.shape[0]
    slots_tile = density.shape[1]
    col_count = lax.axis_size("col")
    col_id = lax.axis_index("col")
    layer_id = lax.axis_index("layer")
    image_of = jnp.zeros((extent,), jnp.int32).at[position].set(jnp.arange(extent, dtype=jnp.int32))
    base = position[layer_id]
    ks = jnp.arange(CANDIDATES, dtype=jnp.int32)
    cand = image_of[(base + ks) % extent]

    right_payload = picked_transposed(density, cand)
    gathered, gathered_offsets, slot_of, first_step = gather_rows((right_payload, block_offset[cand]))

    col_of_piece = (col_id - jnp.arange(col_count, dtype=jnp.int32)) % col_count
    own_ints = jnp.concatenate([block_offset[layer_id], filter_offset[layer_id]])
    extra = jnp.zeros(density.shape[2:], density.dtype).at[0, : own_ints.shape[0]].set(own_ints.astype(density.dtype))
    own_payload = jnp.concatenate([density[layer_id], extra[None]])
    own_payload, _ = lax.optimization_barrier((own_payload, first_step))
    col_payload = gather_col(own_payload)
    left = col_payload[:, :slots_tile].reshape(-1, *density.shape[2:])
    all_ints = col_payload[:, slots_tile, 0, : own_ints.shape[0]].astype(jnp.int32)
    left_offsets = all_ints[:, :slots_tile].reshape(-1)
    filter_all = all_ints[:, slots_tile:].reshape(-1)
    left_w = (col_of_piece[:, None] * slots_tile + jnp.arange(slots_tile, dtype=jnp.int32)).reshape(-1)

    t_count = slots_tile
    t_all = jnp.arange(t_count, dtype=jnp.int32)
    groups = col_id * slots_tile + t_all
    filter_own = filter_offset[layer_id].reshape(t_count, -1)
    target = groups[:, None] * extent + image_of[(base + filter_own) % extent]

    def right_columns(slot_index, k_index):
        offsets = gathered_offsets[slot_index, k_index]
        physical = (position[cand[k_index]][:, None] + offsets) % extent
        return groups[None, :] * extent + image_of[physical]

    def masked_right(slot_index, k_index):
        blocks = gathered[slot_index[None, :], k_index[None, :], t_all[:, None]]
        match = right_columns(slot_index, k_index).T[:, None, :] == target[:, :, None]
        return jnp.where(match[..., None, None], blocks[:, None], jnp.zeros((), blocks.dtype))

    square_slot = slot_of[left_w]
    square_right = masked_right(square_slot, left_offsets)
    square = jnp.einsum("wxy,tjwzy->tjxz", left, square_right, preferred_element_type=jnp.float32)

    square_half = square.astype(jnp.bfloat16).reshape(-1, *square.shape[2:])
    per_col = square_half.shape[0]
    square_all = gather_col(square_half).reshape(-1, *square_half.shape[1:])
    v_all = (col_of_piece[:, None] * per_col + jnp.arange(per_col, dtype=jnp.int32)).reshape(-1)
    row_groups = slot_of.shape[0]
    cube_slot = slot_of[v_all // (col_count * per_col // row_groups)]
    cube_right = masked_right(cube_slot, filter_all)
    cube = jnp.einsum("vxy,tjvzy->tjxz", square_all, cube_right, preferred_element_type=jnp.float32)

    result = 3.0 * square - 2.0 * cube
    return result.reshape(1, -1, *result.shape[2:])


def solution(mesh):
    placed = (P("row", "col", None, None), P("row", "col"), P("row", "col"), P())
    return jax.shard_map(
        on_device,
        mesh=mesh,
        in_specs=placed,
        out_specs=P(("row", "layer"), "col", None, None),
        check_vma=False,
    )
```

```python
import jax
import jax.numpy as jnp
from jax import lax
from jax.experimental import pallas as pl
from jax.experimental.pallas import tpu as pltpu
from jax.sharding import PartitionSpec as P

CANDIDATES = 4


def shifted(value, axis, steps):
    count = lax.axis_size(axis)
    pairs = [(source, (source + steps) % count) for source in range(count)]
    return lax.ppermute(value, axis, pairs)


def partner(value, axis):
    count = lax.axis_size(axis)
    return lax.ppermute(value, axis, [(source, source ^ 1) for source in range(count)])


def gather_rows(pair):
    row_count = lax.axis_size("row")
    z_count = row_count // 2
    row_id = lax.axis_index("row")
    z_id = row_id // 2
    x_lo = row_id % 2
    mine = pair
    theirs = partner(pair, "row")
    chunk = tuple(jnp.stack([a, b]) for a, b in zip(mine, theirs))

    def groups_of(z_source):
        z_source = z_source % z_count
        return [2 * z_source + x_lo, 2 * z_source + 1 - x_lo]

    pieces = [chunk]
    owners = groups_of(z_id)
    ahead, behind = chunk, chunk
    first_step = None
    def in_step(carried):
        data, ints = carried
        ints, _ = lax.optimization_barrier((ints, data))
        return data, ints

    for distance in range(1, z_count // 2):
        ahead = shifted(in_step(ahead), "row", 2)
        behind = shifted(in_step(behind), "row", -2)
        first_step = ahead
        pieces += [ahead, behind]
        owners += groups_of(z_id - distance) + groups_of(z_id + distance)
    last_ahead = shifted(tuple(a[:1] for a in in_step(ahead)), "row", 2)
    last_behind = shifted(tuple(b[1:] for b in in_step(behind)), "row", -2)
    pieces += [last_ahead, last_behind]
    owners += groups_of(z_id - z_count // 2)[:1] + groups_of(z_id + z_count // 2)[1:]
    data = jnp.concatenate([p[0] for p in pieces])
    offsets = jnp.concatenate([p[1] for p in pieces])
    owners = jnp.stack(owners).astype(jnp.int32) % row_count
    slot_of = jnp.zeros((row_count,), jnp.int32).at[owners].set(jnp.arange(row_count, dtype=jnp.int32))
    return data, offsets, slot_of, first_step


def gather_col(value):
    count = lax.axis_size("col")
    return jnp.stack([value] + [shifted(value, "col", d) for d in range(1, count)])


def picked_transposed(density, rows):
    slots, edge = density.shape[1], density.shape[2]

    def kernel(rows_ref, x_ref, o_ref):
        for slot in range(slots):
            o_ref[0, slot] = x_ref[0, slot].astype(jnp.float32).T.astype(o_ref.dtype)

    block = (1, slots, edge, edge)
    grid_spec = pltpu.PrefetchScalarGridSpec(
        num_scalar_prefetch=1,
        grid=(rows.shape[0],),
        in_specs=[pl.BlockSpec(block, lambda i, rows_ref: (rows_ref[i], 0, 0, 0))],
        out_specs=pl.BlockSpec(block, lambda i, rows_ref: (i, 0, 0, 0)),
    )
    out_shape = jax.ShapeDtypeStruct((rows.shape[0],) + density.shape[1:], density.dtype)
    return pl.pallas_call(
        kernel,
        out_shape=out_shape,
        grid_spec=grid_spec,
        cost_estimate=pl.CostEstimate(flops=0, bytes_accessed=2 * 2 * rows.shape[0] * slots * edge * edge, transcendentals=0),
    )(rows, density)


def on_device(density, block_offset, filter_offset, position):
    extent = position.shape[0]
    slots_tile = density.shape[1]
    col_count = lax.axis_size("col")
    col_id = lax.axis_index("col")
    layer_id = lax.axis_index("layer")
    image_of = jnp.zeros((extent,), jnp.int32).at[position].set(jnp.arange(extent, dtype=jnp.int32))
    base = position[layer_id]
    ks = jnp.arange(CANDIDATES, dtype=jnp.int32)
    cand = image_of[(base + ks) % extent]

    right_payload = picked_transposed(density, cand)
    gathered, gathered_offsets, slot_of, first_step = gather_rows((right_payload, block_offset[cand]))

    col_of_piece = (col_id - jnp.arange(col_count, dtype=jnp.int32)) % col_count
    own_ints = jnp.concatenate([block_offset[layer_id], filter_offset[layer_id]])
    extra = jnp.zeros(density.shape[2:], density.dtype).at[0, : own_ints.shape[0]].set(own_ints.astype(density.dtype))
    own_payload = jnp.concatenate([density[layer_id], extra[None]])
    own_payload, _ = lax.optimization_barrier((own_payload, first_step))
    col_payload = gather_col(own_payload)
    left = col_payload[:, :slots_tile].reshape(-1, *density.shape[2:])
    all_ints = col_payload[:, slots_tile, 0, : own_ints.shape[0]].astype(jnp.int32)
    left_offsets = all_ints[:, :slots_tile].reshape(-1)
    filter_all = all_ints[:, slots_tile:].reshape(-1)
    left_w = (col_of_piece[:, None] * slots_tile + jnp.arange(slots_tile, dtype=jnp.int32)).reshape(-1)

    t_count = slots_tile
    t_all = jnp.arange(t_count, dtype=jnp.int32)
    groups = col_id * slots_tile + t_all
    filter_own = filter_offset[layer_id].reshape(t_count, -1)
    target = groups[:, None] * extent + image_of[(base + filter_own) % extent]

    def right_columns(slot_index, k_index):
        offsets = gathered_offsets[slot_index, k_index]
        physical = (position[cand[k_index]][:, None] + offsets) % extent
        return groups[None, :] * extent + image_of[physical]

    def masked_right(slot_index, k_index):
        blocks = gathered[slot_index[None, :], k_index[None, :], t_all[:, None]]
        match = right_columns(slot_index, k_index).T[:, None, :] == target[:, :, None]
        return jnp.where(match[..., None, None], blocks[:, None], jnp.zeros((), blocks.dtype))

    square_slot = slot_of[left_w]
    square_right = masked_right(square_slot, left_offsets)
    square = jnp.einsum("wxy,tjwzy->tjxz", left, square_right, preferred_element_type=jnp.float32)

    square_half = square.astype(jnp.bfloat16).reshape(-1, *square.shape[2:])
    per_col = square_half.shape[0]
    square_all = gather_col(square_half).reshape(-1, *square_half.shape[1:])
    v_all = (col_of_piece[:, None] * per_col + jnp.arange(per_col, dtype=jnp.int32)).reshape(-1)
    row_groups = slot_of.shape[0]
    cube_slot = slot_of[v_all // (col_count * per_col // row_groups)]
    cube_right = masked_right(cube_slot, filter_all)
    cube = jnp.einsum("vxy,tjvzy->tjxz", square_all, cube_right, preferred_element_type=jnp.float32)

    result = 3.0 * square - 2.0 * cube
    return result.reshape(1, -1, *result.shape[2:])


def solution(mesh):
    placed = (P("row", "col", None, None), P("row", "col"), P("row", "col"), P())
    return jax.shard_map(
        on_device,
        mesh=mesh,
        in_specs=placed,
        out_specs=P(("row", "layer"), "col", None, None),
        check_vma=False,
    )
```

```python
import jax
import jax.numpy as jnp
from jax import lax
from jax.experimental import pallas as pl
from jax.experimental.pallas import tpu as pltpu
from jax.sharding import PartitionSpec as P

CANDIDATES = 4


def shifted(value, axis, steps):
    count = lax.axis_size(axis)
    pairs = [(source, (source + steps) % count) for source in range(count)]
    return lax.ppermute(value, axis, pairs)


def partner(value, axis):
    count = lax.axis_size(axis)
    return lax.ppermute(value, axis, [(source, source ^ 1) for source in range(count)])


def gather_rows(pair):
    row_count = lax.axis_size("row")
    z_count = row_count // 2
    row_id = lax.axis_index("row")
    z_id = row_id // 2
    x_lo = row_id % 2
    mine = pair
    theirs = partner(pair, "row")
    chunk = tuple(jnp.stack([a, b]) for a, b in zip(mine, theirs))

    def groups_of(z_source):
        z_source = z_source % z_count
        return [2 * z_source + x_lo, 2 * z_source + 1 - x_lo]

    pieces = [chunk]
    owners = groups_of(z_id)
    ahead, behind = chunk, chunk
    first_step = None
    def in_step(carried):
        data, ints = carried
        ints, _ = lax.optimization_barrier((ints, data))
        return data, ints

    for distance in range(1, z_count // 2):
        ahead = shifted(in_step(ahead), "row", 2)
        behind = shifted(in_step(behind), "row", -2)
        first_step = ahead
        pieces += [ahead, behind]
        owners += groups_of(z_id - distance) + groups_of(z_id + distance)
    last_ahead = shifted(tuple(a[:1] for a in in_step(ahead)), "row", 2)
    last_behind = shifted(tuple(b[1:] for b in in_step(behind)), "row", -2)
    pieces += [last_ahead, last_behind]
    owners += groups_of(z_id - z_count // 2)[:1] + groups_of(z_id + z_count // 2)[1:]
    data = jnp.concatenate([p[0] for p in pieces])
    offsets = jnp.concatenate([p[1] for p in pieces])
    owners = jnp.stack(owners).astype(jnp.int32) % row_count
    slot_of = jnp.zeros((row_count,), jnp.int32).at[owners].set(jnp.arange(row_count, dtype=jnp.int32))
    return data, offsets, slot_of, first_step


def gather_col(value):
    count = lax.axis_size("col")
    return jnp.stack([value] + [shifted(value, "col", d) for d in range(1, count)])


def picked_transposed(density, rows):
    slots, edge = density.shape[1], density.shape[2]

    def kernel(rows_ref, x_ref, o_ref):
        for slot in range(slots):
            o_ref[0, slot] = x_ref[0, slot].astype(jnp.float32).T.astype(o_ref.dtype)

    block = (1, slots, edge, edge)
    grid_spec = pltpu.PrefetchScalarGridSpec(
        num_scalar_prefetch=1,
        grid=(rows.shape[0],),
        in_specs=[pl.BlockSpec(block, lambda i, rows_ref: (rows_ref[i], 0, 0, 0))],
        out_specs=pl.BlockSpec(block, lambda i, rows_ref: (i, 0, 0, 0)),
    )
    out_shape = jax.ShapeDtypeStruct((rows.shape[0],) + density.shape[1:], density.dtype)
    return pl.pallas_call(
        kernel,
        out_shape=out_shape,
        grid_spec=grid_spec,
        cost_estimate=pl.CostEstimate(flops=0, bytes_accessed=2 * 2 * rows.shape[0] * slots * edge * edge, transcendentals=0),
    )(rows, density)


def on_device(density, block_offset, filter_offset, position):
    extent = position.shape[0]
    slots_tile = density.shape[1]
    col_count = lax.axis_size("col")
    col_id = lax.axis_index("col")
    layer_id = lax.axis_index("layer")
    image_of = jnp.zeros((extent,), jnp.int32).at[position].set(jnp.arange(extent, dtype=jnp.int32))
    base = position[layer_id]
    ks = jnp.arange(CANDIDATES, dtype=jnp.int32)
    cand = jnp.argmax(position[None, :] == ((base + ks) % extent)[:, None], axis=1).astype(jnp.int32)

    right_payload = picked_transposed(density, cand)
    gathered, gathered_offsets, slot_of, first_step = gather_rows((right_payload, block_offset[cand]))

    col_of_piece = (col_id - jnp.arange(col_count, dtype=jnp.int32)) % col_count
    own_ints = jnp.concatenate([block_offset[layer_id], filter_offset[layer_id]])
    extra = jnp.zeros(density.shape[2:], density.dtype).at[0, : own_ints.shape[0]].set(own_ints.astype(density.dtype))
    own_payload = jnp.concatenate([density[layer_id], extra[None]])
    own_payload, _ = lax.optimization_barrier((own_payload, first_step))
    col_payload = gather_col(own_payload)
    left = col_payload[:, :slots_tile].reshape(-1, *density.shape[2:])
    all_ints = col_payload[:, slots_tile, 0, : own_ints.shape[0]].astype(jnp.int32)
    left_offsets = all_ints[:, :slots_tile].reshape(-1)
    filter_all = all_ints[:, slots_tile:].reshape(-1)
    left_w = (col_of_piece[:, None] * slots_tile + jnp.arange(slots_tile, dtype=jnp.int32)).reshape(-1)

    t_count = slots_tile
    t_all = jnp.arange(t_count, dtype=jnp.int32)
    groups = col_id * slots_tile + t_all
    filter_own = filter_offset[layer_id].reshape(t_count, -1)
    target = groups[:, None] * extent + image_of[(base + filter_own) % extent]

    def right_columns(slot_index, k_index):
        offsets = gathered_offsets[slot_index, k_index]
        physical = (position[cand[k_index]][:, None] + offsets) % extent
        return groups[None, :] * extent + image_of[physical]

    def masked_right(slot_index, k_index):
        blocks = gathered[slot_index[None, :], k_index[None, :], t_all[:, None]]
        match = right_columns(slot_index, k_index).T[:, None, :] == target[:, :, None]
        return jnp.where(match[..., None, None], blocks[:, None], jnp.zeros((), blocks.dtype))

    square_slot = slot_of[left_w]
    square_right = masked_right(square_slot, left_offsets)
    square = jnp.einsum("wxy,tjwzy->tjxz", left, square_right, preferred_element_type=jnp.float32)

    square_half = square.astype(jnp.bfloat16).reshape(-1, *square.shape[2:])
    per_col = square_half.shape[0]
    square_all = gather_col(square_half).reshape(-1, *square_half.shape[1:])
    v_all = (col_of_piece[:, None] * per_col + jnp.arange(per_col, dtype=jnp.int32)).reshape(-1)
    row_groups = slot_of.shape[0]
    cube_slot = slot_of[v_all // (col_count * per_col // row_groups)]
    cube_right = masked_right(cube_slot, filter_all)
    cube = jnp.einsum("vxy,tjvzy->tjxz", square_all, cube_right, preferred_element_type=jnp.float32)

    result = 3.0 * square - 2.0 * cube
    return result.reshape(1, -1, *result.shape[2:])


def solution(mesh):
    placed = (P("row", "col", None, None), P("row", "col"), P("row", "col"), P())
    return jax.shard_map(
        on_device,
        mesh=mesh,
        in_specs=placed,
        out_specs=P(("row", "layer"), "col", None, None),
        check_vma=False,
    )
```

```python
import jax
import jax.numpy as jnp
from jax import lax
from jax.experimental import pallas as pl
from jax.experimental.pallas import tpu as pltpu
from jax.sharding import PartitionSpec as P

CANDIDATES = 4


def shifted(value, axis, steps):
    count = lax.axis_size(axis)
    pairs = [(source, (source + steps) % count) for source in range(count)]
    return lax.ppermute(value, axis, pairs)


def partner(value, axis):
    count = lax.axis_size(axis)
    return lax.ppermute(value, axis, [(source, source ^ 1) for source in range(count)])


def gather_rows(pair):
    row_count = lax.axis_size("row")
    z_count = row_count // 2
    row_id = lax.axis_index("row")
    z_id = row_id // 2
    x_lo = row_id % 2
    mine = pair
    theirs = partner(pair, "row")
    chunk = tuple(jnp.stack([a, b]) for a, b in zip(mine, theirs))

    def groups_of(z_source):
        z_source = z_source % z_count
        return [2 * z_source + x_lo, 2 * z_source + 1 - x_lo]

    pieces = [chunk]
    owners = groups_of(z_id)
    ahead, behind = chunk, chunk
    first_step = None
    def in_step(carried):
        data, ints = carried
        ints, _ = lax.optimization_barrier((ints, data))
        return data, ints

    for distance in range(1, z_count // 2):
        ahead = shifted(in_step(ahead), "row", 2)
        behind = shifted(in_step(behind), "row", -2)
        first_step = ahead
        pieces += [ahead, behind]
        owners += groups_of(z_id - distance) + groups_of(z_id + distance)
    last_ahead = shifted(tuple(a[:1] for a in in_step(ahead)), "row", 2)
    last_behind = shifted(tuple(b[1:] for b in in_step(behind)), "row", -2)
    pieces += [last_ahead, last_behind]
    owners += groups_of(z_id - z_count // 2)[:1] + groups_of(z_id + z_count // 2)[1:]
    data = jnp.concatenate([p[0] for p in pieces])
    offsets = jnp.concatenate([p[1] for p in pieces])
    owners = jnp.stack(owners).astype(jnp.int32) % row_count
    slot_of = jnp.zeros((row_count,), jnp.int32).at[owners].set(jnp.arange(row_count, dtype=jnp.int32))
    return data, offsets, slot_of, first_step


def gather_col(value):
    count = lax.axis_size("col")
    return jnp.stack([value] + [shifted(value, "col", d) for d in range(1, count)])


def picked_transposed(density, rows):
    slots, edge = density.shape[1], density.shape[2]

    def kernel(rows_ref, x_ref, o_ref):
        for slot in range(slots):
            o_ref[0, slot] = x_ref[0, slot].T

    block = (1, slots, edge, edge)
    grid_spec = pltpu.PrefetchScalarGridSpec(
        num_scalar_prefetch=1,
        grid=(rows.shape[0],),
        in_specs=[pl.BlockSpec(block, lambda i, rows_ref: (rows_ref[i], 0, 0, 0))],
        out_specs=pl.BlockSpec(block, lambda i, rows_ref: (i, 0, 0, 0)),
    )
    out_shape = jax.ShapeDtypeStruct((rows.shape[0],) + density.shape[1:], density.dtype)
    return pl.pallas_call(
        kernel,
        out_shape=out_shape,
        grid_spec=grid_spec,
        cost_estimate=pl.CostEstimate(flops=0, bytes_accessed=2 * 2 * rows.shape[0] * slots * edge * edge, transcendentals=0),
    )(rows, density)


def on_device(density, block_offset, filter_offset, position):
    extent = position.shape[0]
    slots_tile = density.shape[1]
    col_count = lax.axis_size("col")
    col_id = lax.axis_index("col")
    layer_id = lax.axis_index("layer")
    image_of = jnp.zeros((extent,), jnp.int32).at[position].set(jnp.arange(extent, dtype=jnp.int32))
    base = position[layer_id]
    ks = jnp.arange(CANDIDATES, dtype=jnp.int32)
    cand = jnp.argmax(position[None, :] == ((base + ks) % extent)[:, None], axis=1).astype(jnp.int32)

    right_payload = picked_transposed(density, cand)
    gathered, gathered_offsets, slot_of, first_step = gather_rows((right_payload, block_offset[cand]))

    col_of_piece = (col_id - jnp.arange(col_count, dtype=jnp.int32)) % col_count
    own_ints = jnp.concatenate([block_offset[layer_id], filter_offset[layer_id]])
    extra = jnp.zeros(density.shape[2:], density.dtype).at[0, : own_ints.shape[0]].set(own_ints.astype(density.dtype))
    own_payload = jnp.concatenate([density[layer_id], extra[None]])
    own_payload, _ = lax.optimization_barrier((own_payload, first_step))
    col_payload = gather_col(own_payload)
    left = col_payload[:, :slots_tile].reshape(-1, *density.shape[2:])
    all_ints = col_payload[:, slots_tile, 0, : own_ints.shape[0]].astype(jnp.int32)
    left_offsets = all_ints[:, :slots_tile].reshape(-1)
    filter_all = all_ints[:, slots_tile:].reshape(-1)
    left_w = (col_of_piece[:, None] * slots_tile + jnp.arange(slots_tile, dtype=jnp.int32)).reshape(-1)

    t_count = slots_tile
    t_all = jnp.arange(t_count, dtype=jnp.int32)
    groups = col_id * slots_tile + t_all
    filter_own = filter_offset[layer_id].reshape(t_count, -1)
    target = groups[:, None] * extent + image_of[(base + filter_own) % extent]

    def right_columns(slot_index, k_index):
        offsets = gathered_offsets[slot_index, k_index]
        physical = (position[cand[k_index]][:, None] + offsets) % extent
        return groups[None, :] * extent + image_of[physical]

    def masked_right(slot_index, k_index):
        blocks = gathered[slot_index[None, :], k_index[None, :], t_all[:, None]]
        match = right_columns(slot_index, k_index).T[:, None, :] == target[:, :, None]
        return jnp.where(match[..., None, None], blocks[:, None], jnp.zeros((), blocks.dtype))

    square_slot = slot_of[left_w]
    square_right = masked_right(square_slot, left_offsets)
    square = jnp.einsum("wxy,tjwzy->tjxz", left, square_right, preferred_element_type=jnp.float32)

    square_half = square.astype(jnp.bfloat16).reshape(-1, *square.shape[2:])
    per_col = square_half.shape[0]
    square_all = gather_col(square_half).reshape(-1, *square_half.shape[1:])
    v_all = (col_of_piece[:, None] * per_col + jnp.arange(per_col, dtype=jnp.int32)).reshape(-1)
    row_groups = slot_of.shape[0]
    cube_slot = slot_of[v_all // (col_count * per_col // row_groups)]
    cube_right = masked_right(cube_slot, filter_all)
    cube = jnp.einsum("vxy,tjvzy->tjxz", square_all, cube_right, preferred_element_type=jnp.float32)

    result = 3.0 * square - 2.0 * cube
    return result.reshape(1, -1, *result.shape[2:])


def solution(mesh):
    placed = (P("row", "col", None, None), P("row", "col"), P("row", "col"), P())
    return jax.shard_map(
        on_device,
        mesh=mesh,
        in_specs=placed,
        out_specs=P(("row", "layer"), "col", None, None),
        check_vma=False,
    )
```
